128 devices in a mesh: prow: 8 (over x, y_lo), pcol: 16 (over z, y_hi, core).
Axes of the slice: x: 4, y: 4 (y_hi: 2, y_lo: 2; y = y_hi * 2 + y_lo), z: 4, core: 2. Of those that a mesh axis runs over, the one named last changes fastest.
Arguments:
- trailing: bfloat16 [16384, 16384], P('prow', 'pcol'), may hold values from -6 to 6
- lower_slot_blocks: bfloat16 [16, 8192, 128], P('pcol', 'prow'), may hold values from -6 to 6
- l_rows: int32 [16, 64], P(None, 'prow'), may hold values from -1 to 127, as said below
- d_inv: bfloat16 [16, 128, 128], P('pcol'), may hold values from -0.5 to 0.5
- u_panel: bfloat16 [2048, 16384], P('prow', 'pcol'), may hold values from -0.125 to 0.125
- pivot: int32 [16, 128], P('prow'), may hold values from 0 to 127, each once within a row
Outputs:
- schur: bfloat16 [16384, 16384], P('prow', 'pcol')
The draws below stay inside these ranges and needn't reach their ends.
Inputs may be any that keep to these rules, and one draw needn't show every extreme that they name: `l_rows`: for each panel, the entries are taken in aligned groups of 8, group g belonging to block rows g * 16 to (g + 1) * 16 - 1: the live entries of a group are distinct block rows of that range and come first, followed by -1; a group holds 4 to 8 live entries, and in every panel some group holds exactly 8.
All inputs are finite; a program needn't handle non-finite values.
Results may differ from the reference program's by a relative error of at most 0.0033.
Values may be sent and summed in bfloat16 or wider, within the bound.
No kernel may reach another device: no remote copies, remote signals or barrier semaphores. Data moves between devices by JAX's collectives and lax.ppermute only.
A program may use at most 64 MiB of HBM per device.

```python
import jax
import jax.numpy as jnp
from jax import lax

SUPERNODE_WIDTH = 128
RB_DEV = 16
CB_DEV = 8
PANEL_COUNT = 16
NZ = 8
LOWER_SLOT_COUNT = 64
NBR = 128
NBC = 128


def draw_l_rows(key, part):
    groups = NBR // RB_DEV
    key_perm, key_count = jax.random.split(key)
    subkeys = jax.random.split(key_perm, PANEL_COUNT * groups)
    orders = jax.vmap(lambda subkey: jax.random.permutation(subkey, RB_DEV))(subkeys)
    orders = orders.reshape(PANEL_COUNT, groups, RB_DEV)[:, :, :NZ].astype(jnp.int32)
    starts = (jnp.arange(groups, dtype=jnp.int32) * RB_DEV)[None, :, None]
    counts = jax.random.randint(key_count, (PANEL_COUNT, groups), NZ // 2, NZ + 1)
    full_group = (jnp.arange(PANEL_COUNT, dtype=jnp.int32) % groups)[:, None]
    counts = jnp.where(jnp.arange(groups, dtype=jnp.int32)[None, :] == full_group, NZ, counts)
    is_live = jnp.arange(NZ, dtype=jnp.int32)[None, None, :] < counts[:, :, None]
    entries = jnp.where(is_live, orders + starts, -1)
    return entries.reshape(PANEL_COUNT, groups * NZ).astype(jnp.int32)


def shard_levels(key, dims, shards, smallest, largest):
    def one(axis_at, blocks):
        steps = jax.random.uniform(jax.random.fold_in(jax.random.fold_in(key, 6), axis_at), (blocks,), jnp.float32, smallest / len(shards), largest / len(shards))
        return jnp.repeat(jnp.exp(steps), dims[axis_at] // blocks).reshape((-1,) + (1,) * (len(dims) - axis_at - 1))

    loudness = one(*shards[0])
    for cut in shards[1:]:
        loudness = loudness * one(*cut)
    return loudness


def scatter_about(key, dims, width, limit, shards=(), held_as=jnp.bfloat16):
    loudness = shard_levels(key, dims, shards, -0.22, 0.18) if shards else 1.0
    drawn = jax.random.normal(key, dims, jnp.float32) * width * loudness
    return jnp.minimum(jnp.maximum(drawn, -limit), limit).astype(held_as)


def setup_inputs(seed: int = 0) -> dict:
    key_list = jax.random.split(jax.random.key(seed), 7)
    return {
        "trailing": scatter_about(key_list[0], (NBR * SUPERNODE_WIDTH, NBC * SUPERNODE_WIDTH), 1.0, 6.0, ((0, 8), (1, 16))),
        "lower_slot_blocks": scatter_about(key_list[1], (PANEL_COUNT, LOWER_SLOT_COUNT * SUPERNODE_WIDTH, SUPERNODE_WIDTH), 1.0, 6.0, ((0, 16), (1, 8))),
        "l_rows": draw_l_rows(jax.random.fold_in(key_list[6], 71), 0),
        "d_inv": scatter_about(key_list[3], (PANEL_COUNT, SUPERNODE_WIDTH, SUPERNODE_WIDTH), SUPERNODE_WIDTH ** -0.5, 0.5, ((0, 16),)),
        "u_panel": scatter_about(key_list[4], (PANEL_COUNT * SUPERNODE_WIDTH, NBC * SUPERNODE_WIDTH), (PANEL_COUNT * SUPERNODE_WIDTH) ** -0.5, 0.125, ((0, 8), (1, 16))),
        "pivot": jax.vmap(lambda own: jax.random.permutation(own, SUPERNODE_WIDTH))(jax.random.split(key_list[5], PANEL_COUNT)).reshape((PANEL_COUNT, SUPERNODE_WIDTH)).astype(jnp.int32),
    }


def reference(trailing, lower_slot_blocks, l_rows, d_inv, u_panel, pivot):
    update_fragments = lower_slot_blocks.reshape(PANEL_COUNT, LOWER_SLOT_COUNT, SUPERNODE_WIDTH, SUPERNODE_WIDTH).astype(jnp.float32)
    scaled = jnp.einsum("ksab,kbc->ksac", update_fragments, d_inv.astype(jnp.float32)).astype(jnp.bfloat16)
    levels = jnp.arange(NBR, dtype=jnp.int32)
    onehot = (l_rows[:, None, :] == levels[None, :, None]).astype(jnp.float32)
    dense_lower = jnp.einsum("kis,ksac->iakc", onehot, scaled.astype(jnp.float32))
    dense_lower = dense_lower.reshape(NBR * SUPERNODE_WIDTH, PANEL_COUNT * SUPERNODE_WIDTH).astype(jnp.bfloat16)
    upper_rows = u_panel.reshape(PANEL_COUNT, SUPERNODE_WIDTH, NBC * SUPERNODE_WIDTH)
    u_pivoted = jax.vmap(lambda matrix, ordering: matrix[ordering])(upper_rows, pivot).reshape(PANEL_COUNT * SUPERNODE_WIDTH, NBC * SUPERNODE_WIDTH)
    col_width = CB_DEV * SUPERNODE_WIDTH

    def column_block(column_index):
        first_col = column_index * col_width
        upper_portion = lax.dynamic_slice_in_dim(u_pivoted, first_col, col_width, 1)
        t_part = lax.dynamic_slice_in_dim(trailing, first_col, col_width, 1)
        update = jnp.dot(dense_lower, upper_portion, preferred_element_type=jnp.float32)
        return (t_part.astype(jnp.float32) - update).astype(jnp.bfloat16)

    parts_out = lax.map(column_block, jnp.arange(NBC // CB_DEV, dtype=jnp.int32))
    return jnp.transpose(parts_out, (1, 0, 2)).reshape(NBR * SUPERNODE_WIDTH, NBC * SUPERNODE_WIDTH)
```

```python
import jax
import jax.numpy as jnp
from jax import lax
from jax.sharding import PartitionSpec as P


def per_device(trailing, lower_slot_blocks, l_rows, d_inv, u_panel, pivot):
    side = d_inv.shape[-1]
    row_blocks = trailing.shape[0] // side
    col_count = trailing.shape[1]
    panels, slot_count = l_rows.shape
    n_rows = lax.axis_size("prow")
    u_own = pivot.shape[0]

    fragments = lower_slot_blocks.reshape(-1, slot_count, side, side)
    scaled = jnp.einsum(
        "ksab,kbc->ksac", fragments, d_inv, preferred_element_type=jnp.float32
    ).astype(jnp.bfloat16)
    scaled_all = lax.all_gather(scaled, "pcol", axis=0, tiled=True)

    upper_rows = u_panel.reshape(-1, side, col_count)
    pivoted = jax.vmap(lambda matrix, ordering: matrix[ordering])(upper_rows, pivot).reshape(
        -1, col_count
    )
    me = lax.axis_index("prow")
    pieces = [pivoted]
    for shift in range(1, n_rows):
        pieces.append(
            lax.ppermute(pivoted, "prow", [(i, (i + shift) % n_rows) for i in range(n_rows)])
        )
    u_whole = jnp.concatenate(pieces, axis=0)

    sources = (me - jnp.arange(n_rows, dtype=jnp.int32)) % n_rows
    order = (sources[:, None] * u_own + jnp.arange(u_own, dtype=jnp.int32)[None, :]).reshape(-1)

    local_ids = jnp.where(l_rows >= 0, l_rows - me * row_blocks, -1)
    levels = jnp.arange(row_blocks, dtype=jnp.int32)
    panel_ids = jnp.arange(panels, dtype=jnp.int32)
    hit_row = local_ids[None, None, :, :] == levels[:, None, None, None]
    hit_panel = panel_ids[None, None, :, None] == order[None, :, None, None]
    onehot = (hit_row & hit_panel).astype(jnp.bfloat16)
    dense_lower = jnp.einsum(
        "ipks,ksac->iapc", onehot, scaled_all, preferred_element_type=jnp.float32
    ).astype(jnp.bfloat16)
    dense_lower = dense_lower.reshape(row_blocks * side, panels * side)

    running = jnp.dot(dense_lower, u_whole, preferred_element_type=jnp.float32)
    return (trailing.astype(jnp.float32) - running).astype(jnp.bfloat16)


def solution(mesh):
    placed = (
        P("prow", "pcol"),
        P("pcol", "prow", None),
        P(None, "prow"),
        P("pcol", None, None),
        P("prow", "pcol"),
        P("prow", None),
    )
    return jax.shard_map(
        per_device, mesh=mesh, in_specs=placed, out_specs=P("prow", "pcol"), check_vma=False
    )
```

```python
import jax
import jax.numpy as jnp
from jax import lax
from jax.sharding import PartitionSpec as P


def per_device(trailing, lower_slot_blocks, l_rows, d_inv, u_panel, pivot):
    side = d_inv.shape[-1]
    row_blocks = trailing.shape[0] // side
    col_count = trailing.shape[1]
    panels, slot_count = l_rows.shape
    n_rows = lax.axis_size("prow")
    u_own = pivot.shape[0]

    fragments = lower_slot_blocks.reshape(-1, slot_count, side, side)
    scaled = jnp.einsum(
        "ksab,kbc->ksac", fragments, d_inv, preferred_element_type=jnp.float32
    ).astype(jnp.bfloat16)
    scaled = jnp.concatenate([scaled, jnp.zeros_like(scaled[:, :1])], axis=1)
    scaled_all = lax.all_gather(scaled, "pcol", axis=0, tiled=True)

    upper_rows = u_panel.reshape(-1, side, col_count)
    lanes = jnp.arange(side, dtype=jnp.int32)
    permuting = (pivot[:, :, None] == lanes[None, None, :]).astype(jnp.bfloat16)
    pivoted = jnp.einsum(
        "kpq,kqn->kpn", permuting, upper_rows, preferred_element_type=jnp.float32
    ).astype(jnp.bfloat16).reshape(-1, col_count)
    me = lax.axis_index("prow")
    pieces = [pivoted]
    for shift in range(1, n_rows):
        pieces.append(
            lax.ppermute(pivoted, "prow", [(i, (i + shift) % n_rows) for i in range(n_rows)])
        )
    u_whole = jnp.concatenate(pieces, axis=0)

    sources = (me - jnp.arange(n_rows, dtype=jnp.int32)) % n_rows
    order = (sources[:, None] * u_own + jnp.arange(u_own, dtype=jnp.int32)[None, :]).reshape(-1)

    local_ids = jnp.where(l_rows >= 0, l_rows - me * row_blocks, -1)
    levels = jnp.arange(row_blocks, dtype=jnp.int32)
    hit = local_ids[:, None, :] == levels[None, :, None]
    present = jnp.any(hit, axis=-1)
    slot_of = jnp.sum(jnp.where(hit, jnp.arange(slot_count, dtype=jnp.int32), 0), axis=-1)
    panel_at = jnp.broadcast_to(order[:, None], (panels, row_blocks))
    slot_at = jnp.where(present[order], slot_of[order], slot_count)
    indices = jnp.stack([panel_at, slot_at], axis=-1)
    numbers = lax.GatherDimensionNumbers(
        offset_dims=(2, 3), collapsed_slice_dims=(0, 1), start_index_map=(0, 1)
    )
    blocks = lax.gather(
        scaled_all,
        indices,
        numbers,
        slice_sizes=(1, 1, side, side),
        mode=lax.GatherScatterMode.PROMISE_IN_BOUNDS,
    )

    running = jnp.einsum(
        "piac,pcn->ian", blocks, u_whole.reshape(panels, side, col_count),
        preferred_element_type=jnp.float32,
    ).reshape(row_blocks * side, col_count)
    return (trailing.astype(jnp.float32) - running).astype(jnp.bfloat16)


def solution(mesh):
    placed = (
        P("prow", "pcol"),
        P("pcol", "prow", None),
        P(None, "prow"),
        P("pcol", None, None),
        P("prow", "pcol"),
        P("prow", None),
    )
    return jax.shard_map(
        per_device, mesh=mesh, in_specs=placed, out_specs=P("prow", "pcol"), check_vma=False
    )
```

```python
import jax
import jax.numpy as jnp
from jax import lax
from jax.sharding import PartitionSpec as P


def per_device(trailing, lower_slot_blocks, l_rows, d_inv, u_panel, pivot):
    side = d_inv.shape[-1]
    row_blocks = trailing.shape[0] // side
    col_count = trailing.shape[1]
    panels, slot_count = l_rows.shape
    n_rows = lax.axis_size("prow")
    u_own = pivot.shape[0]

    fragments = lower_slot_blocks.reshape(-1, slot_count, side, side)
    scaled = jnp.einsum(
        "ksab,kbc->ksac", fragments, d_inv, preferred_element_type=jnp.float32
    ).astype(jnp.bfloat16)
    scaled = jnp.concatenate([scaled, jnp.zeros_like(scaled[:, :1])], axis=1)
    n_cols = lax.axis_size("pcol")
    col = lax.axis_index("pcol")
    held = [scaled]
    for shift in range(1, n_cols // 2):
        held.append(
            lax.ppermute(
                scaled, "pcol", [(i, (i + 2 * shift) % n_cols) for i in range(n_cols)]
            )
        )
    sibling = [(i, i ^ 1) for i in range(n_cols)]
    swapped = [lax.ppermute(piece, "pcol", sibling) for piece in held]
    scaled_all = jnp.concatenate(held + swapped, axis=0)
    steps = jnp.arange(n_cols // 2, dtype=jnp.int32)
    lower_order = jnp.concatenate([(col - 2 * steps) % n_cols, ((col ^ 1) - 2 * steps) % n_cols])
    panel_ids = jnp.arange(panels, dtype=jnp.int32)
    lower_pos = jnp.sum(
        jnp.where(lower_order[None, :] == panel_ids[:, None], panel_ids[None, :], 0), axis=1
    )

    upper_rows = u_panel.reshape(-1, side, col_count)
    lanes = jnp.arange(side, dtype=jnp.int32)
    permuting = (pivot[:, :, None] == lanes[None, None, :]).astype(jnp.bfloat16)
    pivoted = jnp.einsum(
        "kpq,kqn->kpn", permuting, upper_rows, preferred_element_type=jnp.float32
    ).astype(jnp.bfloat16).reshape(-1, col_count)
    me = lax.axis_index("prow")
    pieces = [pivoted]
    for shift in range(1, n_rows):
        pieces.append(
            lax.ppermute(pivoted, "prow", [(i, (i + shift) % n_rows) for i in range(n_rows)])
        )
    u_whole = jnp.concatenate(pieces, axis=0)

    sources = (me - jnp.arange(n_rows, dtype=jnp.int32)) % n_rows
    order = (sources[:, None] * u_own + jnp.arange(u_own, dtype=jnp.int32)[None, :]).reshape(-1)

    local_ids = jnp.where(l_rows >= 0, l_rows - me * row_blocks, -1)
    levels = jnp.arange(row_blocks, dtype=jnp.int32)
    hit = local_ids[:, None, :] == levels[None, :, None]
    present = jnp.any(hit, axis=-1)
    slot_of = jnp.sum(jnp.where(hit, jnp.arange(slot_count, dtype=jnp.int32), 0), axis=-1)
    panel_at = jnp.broadcast_to(lower_pos[order][:, None], (panels, row_blocks))
    slot_at = jnp.where(present[order], slot_of[order], slot_count)
    indices = jnp.stack([panel_at, slot_at], axis=-1)
    numbers = lax.GatherDimensionNumbers(
        offset_dims=(2, 3), collapsed_slice_dims=(0, 1), start_index_map=(0, 1)
    )
    blocks = lax.gather(
        scaled_all,
        indices,
        numbers,
        slice_sizes=(1, 1, side, side),
        mode=lax.GatherScatterMode.PROMISE_IN_BOUNDS,
    )

    running = jnp.einsum(
        "piac,pcn->ian", blocks, u_whole.reshape(panels, side, col_count),
        preferred_element_type=jnp.float32,
    ).reshape(row_blocks * side, col_count)
    return (trailing.astype(jnp.float32) - running).astype(jnp.bfloat16)


def solution(mesh):
    placed = (
        P("prow", "pcol"),
        P("pcol", "prow", None),
        P(None, "prow"),
        P("pcol", None, None),
        P("prow", "pcol"),
        P("prow", None),
    )
    return jax.shard_map(
        per_device, mesh=mesh, in_specs=placed, out_specs=P("prow", "pcol"), check_vma=False
    )
```

```python
import functools

import jax
import jax.numpy as jnp
from jax import lax
from jax.experimental import pallas as pl
from jax.experimental.pallas import tpu as pltpu
from jax.sharding import PartitionSpec as P


def _update_kernel(n_u, n_l, rows, table_ref, trailing_ref, *refs):
    u_hbm = refs[:n_u]
    l_hbm = refs[n_u:n_u + n_l]
    out_ref = refs[n_u + n_l]
    u_scr, l_scr, lrow, sems = refs[n_u + n_l + 1:]
    side = l_scr.shape[-1]
    held = l_scr.shape[0] // n_l
    u_rows = u_scr.shape[0] // n_u
    step = pl.program_id(0)

    @pl.when(step == 0)
    def _():
        copies = [
            pltpu.make_async_copy(u_hbm[j], u_scr.at[pl.ds(j * u_rows, u_rows)], sems.at[j])
            for j in range(n_u)
        ] + [
            pltpu.make_async_copy(l_hbm[j], l_scr.at[pl.ds(j * held, held)], sems.at[n_u + j])
            for j in range(n_l)
        ]
        for c in copies:
            c.start()
        for c in copies:
            c.wait()

    groups = rows // side
    panels = lrow.shape[1] // side
    for r in range(groups):
        for p in range(panels):
            idx = table_ref[p, step * groups + r]
            lrow[r * side:(r + 1) * side, p * side:(p + 1) * side] = l_scr[idx]
    tile = 256
    for n in range(out_ref.shape[1] // tile):
        cols = slice(n * tile, (n + 1) * tile)
        acc = jnp.dot(lrow[...], u_scr[:, cols], preferred_element_type=jnp.float32)
        out_ref[:, cols] = (trailing_ref[:, cols].astype(jnp.float32) - acc).astype(out_ref.dtype)


def fused_update(table, trailing, u_pieces, l_pieces):
    rows = 256
    side = l_pieces[0].shape[-1]
    held = l_pieces[0].shape[0]
    n_u, n_l = len(u_pieces), len(l_pieces)
    m, n = trailing.shape
    u_rows = u_pieces[0].shape[0]
    k = n_u * u_rows
    kernel = functools.partial(_update_kernel, n_u, n_l, rows)
    any_spec = pl.BlockSpec(memory_space=pl.ANY)
    grid_spec = pltpu.PrefetchScalarGridSpec(
        num_scalar_prefetch=1,
        grid=(m // rows,),
        in_specs=[pl.BlockSpec((rows, n), lambda g, t: (g, 0))] + [any_spec] * (n_u + n_l),
        out_specs=pl.BlockSpec((rows, n), lambda g, t: (g, 0)),
        scratch_shapes=[
            pltpu.VMEM((k, n), u_pieces[0].dtype),
            pltpu.VMEM((n_l * held, side, side), l_pieces[0].dtype),
            pltpu.VMEM((rows, k), l_pieces[0].dtype),
            pltpu.SemaphoreType.DMA((n_u + n_l,)),
        ],
    )
    return pl.pallas_call(
        kernel,
        grid_spec=grid_spec,
        out_shape=jax.ShapeDtypeStruct((m, n), trailing.dtype),
        compiler_params=pltpu.CompilerParams(
            dimension_semantics=("arbitrary",), vmem_limit_bytes=48 * 1024 * 1024
        ),
        cost_estimate=pl.CostEstimate(
            flops=2 * m * k * n, transcendentals=0, bytes_accessed=2 * (2 * m * n + k * n + n_l * held * side * side)
        ),
    )(table, trailing, *u_pieces, *l_pieces)


def per_device(trailing, lower_slot_blocks, l_rows, d_inv, u_panel, pivot):
    side = d_inv.shape[-1]
    row_blocks = trailing.shape[0] // side
    col_count = trailing.shape[1]
    panels, slot_count = l_rows.shape
    n_rows = lax.axis_size("prow")
    u_own = pivot.shape[0]

    fragments = lower_slot_blocks.reshape(-1, slot_count, side, side)
    scaled = jnp.einsum(
        "ksab,kbc->ksac", fragments, d_inv, preferred_element_type=jnp.float32
    ).astype(jnp.bfloat16)
    scaled = jnp.concatenate([scaled, jnp.zeros_like(scaled[:, :1])], axis=1)
    n_cols = lax.axis_size("pcol")
    col = lax.axis_index("pcol")
    held = [scaled]
    for shift in range(1, n_cols // 2):
        held.append(
            lax.ppermute(
                scaled, "pcol", [(i, (i + 2 * shift) % n_cols) for i in range(n_cols)]
            )
        )
    sibling = [(i, i ^ 1) for i in range(n_cols)]
    swapped = [lax.ppermute(piece, "pcol", sibling) for piece in held]
    steps = jnp.arange(n_cols // 2, dtype=jnp.int32)
    lower_order = jnp.concatenate([(col - 2 * steps) % n_cols, ((col ^ 1) - 2 * steps) % n_cols])
    panel_ids = jnp.arange(panels, dtype=jnp.int32)
    lower_pos = jnp.sum(
        jnp.where(lower_order[None, :] == panel_ids[:, None], panel_ids[None, :], 0), axis=1
    )

    upper_rows = u_panel.reshape(-1, side, col_count)
    lanes = jnp.arange(side, dtype=jnp.int32)
    permuting = (pivot[:, :, None] == lanes[None, None, :]).astype(jnp.bfloat16)
    pivoted = jnp.einsum(
        "kpq,kqn->kpn", permuting, upper_rows, preferred_element_type=jnp.float32
    ).astype(jnp.bfloat16).reshape(-1, col_count)
    me = lax.axis_index("prow")
    pieces = [pivoted]
    for shift in range(1, n_rows):
        pieces.append(
            lax.ppermute(pivoted, "prow", [(i, (i + shift) % n_rows) for i in range(n_rows)])
        )

    sources = (me - jnp.arange(n_rows, dtype=jnp.int32)) % n_rows
    order = (sources[:, None] * u_own + jnp.arange(u_own, dtype=jnp.int32)[None, :]).reshape(-1)

    local_ids = jnp.where(l_rows >= 0, l_rows - me * row_blocks, -1)
    levels = jnp.arange(row_blocks, dtype=jnp.int32)
    hit = local_ids[:, None, :] == levels[None, :, None]
    present = jnp.any(hit, axis=-1)
    slot_of = jnp.sum(jnp.where(hit, jnp.arange(slot_count, dtype=jnp.int32), 0), axis=-1)
    slot_at = jnp.where(present[order], slot_of[order], slot_count)
    table = lower_pos[order][:, None] * (slot_count + 1) + slot_at
    l_pieces = [piece.reshape(slot_count + 1, side, side) for piece in held + swapped]
    return fused_update(table, trailing, pieces, l_pieces)


def solution(mesh):
    placed = (
        P("prow", "pcol"),
        P("pcol", "prow", None),
        P(None, "prow"),
        P("pcol", None, None),
        P("prow", "pcol"),
        P("prow", None),
    )
    return jax.shard_map(
        per_device, mesh=mesh, in_specs=placed, out_specs=P("prow", "pcol"), check_vma=False
    )
```

```python
import functools

import jax
import jax.numpy as jnp
from jax import lax
from jax.experimental import pallas as pl
from jax.experimental.pallas import tpu as pltpu
from jax.sharding import PartitionSpec as P


def _update_kernel(u_starts, n_l, rows, table_ref, trailing_ref, *refs):
    n_u = len(u_starts) - 1
    u_hbm = refs[:n_u]
    l_hbm = refs[n_u:n_u + n_l]
    out_ref = refs[n_u + n_l]
    u_scr, l_scr, lrow, sems = refs[n_u + n_l + 1:]
    side = l_scr.shape[-1]
    held = l_scr.shape[0] // n_l
    step = pl.program_id(0)

    @pl.when(step == 0)
    def _():
        copies = [
            pltpu.make_async_copy(
                u_hbm[j],
                u_scr.at[pl.ds(u_starts[j], u_starts[j + 1] - u_starts[j])],
                sems.at[j],
            )
            for j in range(n_u)
        ] + [
            pltpu.make_async_copy(l_hbm[j], l_scr.at[pl.ds(j * held, held)], sems.at[n_u + j])
            for j in range(n_l)
        ]
        for c in copies:
            c.start()
        for c in copies:
            c.wait()

    groups = rows // side
    panels = lrow.shape[1] // side
    for r in range(groups):
        for p in range(panels):
            idx = table_ref[p, step * groups + r]
            lrow[r * side:(r + 1) * side, p * side:(p + 1) * side] = l_scr[idx]
    tile = 256
    for n in range(out_ref.shape[1] // tile):
        cols = slice(n * tile, (n + 1) * tile)
        acc = jnp.dot(lrow[...], u_scr[:, cols], preferred_element_type=jnp.float32)
        out_ref[:, cols] = (trailing_ref[:, cols].astype(jnp.float32) - acc).astype(out_ref.dtype)


def fused_update(table, trailing, u_pieces, l_pieces):
    rows = 256
    side = l_pieces[0].shape[-1]
    held = l_pieces[0].shape[0]
    n_u, n_l = len(u_pieces), len(l_pieces)
    m, n = trailing.shape
    u_starts = [0]
    for piece in u_pieces:
        u_starts.append(u_starts[-1] + piece.shape[0])
    k = u_starts[-1]
    kernel = functools.partial(_update_kernel, tuple(u_starts), n_l, rows)
    any_spec = pl.BlockSpec(memory_space=pl.ANY)
    grid_spec = pltpu.PrefetchScalarGridSpec(
        num_scalar_prefetch=1,
        grid=(m // rows,),
        in_specs=[pl.BlockSpec((rows, n), lambda g, t: (g, 0))] + [any_spec] * (n_u + n_l),
        out_specs=pl.BlockSpec((rows, n), lambda g, t: (g, 0)),
        scratch_shapes=[
            pltpu.VMEM((k, n), u_pieces[0].dtype),
            pltpu.VMEM((n_l * held, side, side), l_pieces[0].dtype),
            pltpu.VMEM((rows, k), l_pieces[0].dtype),
            pltpu.SemaphoreType.DMA((n_u + n_l,)),
        ],
    )
    return pl.pallas_call(
        kernel,
        grid_spec=grid_spec,
        out_shape=jax.ShapeDtypeStruct((m, n), trailing.dtype),
        compiler_params=pltpu.CompilerParams(
            dimension_semantics=("arbitrary",), vmem_limit_bytes=48 * 1024 * 1024
        ),
        cost_estimate=pl.CostEstimate(
            flops=2 * m * k * n, transcendentals=0, bytes_accessed=2 * (2 * m * n + k * n + n_l * held * side * side)
        ),
    )(table, trailing, *u_pieces, *l_pieces)


def per_device(trailing, lower_slot_blocks, l_rows, d_inv, u_panel, pivot):
    side = d_inv.shape[-1]
    row_blocks = trailing.shape[0] // side
    col_count = trailing.shape[1]
    panels, slot_count = l_rows.shape
    n_rows = lax.axis_size("prow")
    u_own = pivot.shape[0]

    fragments = lower_slot_blocks.reshape(-1, slot_count, side, side)
    scaled = jnp.einsum(
        "ksab,kbc->ksac", fragments, d_inv, preferred_element_type=jnp.float32
    ).astype(jnp.bfloat16)
    scaled = jnp.concatenate([scaled, jnp.zeros_like(scaled[:, :1])], axis=1)
    n_cols = lax.axis_size("pcol")
    col = lax.axis_index("pcol")
    z_step = 4
    crossed = lax.ppermute(scaled, "pcol", [(i, i ^ 2) for i in range(n_cols)])
    held = [scaled, crossed]
    for base in (scaled, crossed):
        for hop in range(1, n_cols // z_step):
            held.append(
                lax.ppermute(
                    base, "pcol", [(i, (i + z_step * hop) % n_cols) for i in range(n_cols)]
                )
            )
    swapped = [lax.ppermute(piece, "pcol", [(i, i ^ 1) for i in range(n_cols)]) for piece in held]

    def lower_sources(c):
        hops = [(c - z_step * hop) % n_cols for hop in range(1, n_cols // z_step)]
        return [c, c ^ 2] + hops + [h ^ 2 for h in hops]

    lower_order = jnp.stack(lower_sources(col) + lower_sources(col ^ 1))
    panel_ids = jnp.arange(panels, dtype=jnp.int32)
    lower_pos = jnp.sum(
        jnp.where(lower_order[None, :] == panel_ids[:, None], panel_ids[None, :], 0), axis=1
    )

    upper_rows = u_panel.reshape(-1, side, col_count)
    lanes = jnp.arange(side, dtype=jnp.int32)
    permuting = (pivot[:, :, None] == lanes[None, None, :]).astype(jnp.bfloat16)
    pivoted = jnp.einsum(
        "kpq,kqn->kpn", permuting, upper_rows, preferred_element_type=jnp.float32
    ).astype(jnp.bfloat16).reshape(-1, col_count)
    me = lax.axis_index("prow")
    x_step = 2
    half = side

    def shifted(piece, by):
        return lax.ppermute(piece, "prow", [(i, (i + by) % n_rows) for i in range(n_rows)])

    crossed_u = lax.ppermute(pivoted, "prow", [(i, i ^ 1) for i in range(n_rows)])
    pieces = []
    panel_list = []
    for base, flip in ((pivoted, 0), (crossed_u, 1)):
        right = shifted(base, x_step)
        left = shifted(base, -x_step)
        far_a = shifted(right[:half], x_step)
        far_b = shifted(left[half:], -x_step)
        pieces += [base, right, left, far_a, far_b]
        source = me ^ flip
        src_r = ((me - x_step) % n_rows) ^ flip
        src_l = ((me + x_step) % n_rows) ^ flip
        src_f = ((me + 2 * x_step) % n_rows) ^ flip
        for q in (source, src_r, src_l):
            panel_list += [u_own * q, u_own * q + 1]
        panel_list += [u_own * src_f, u_own * src_f + 1]
    order = jnp.stack(panel_list)

    local_ids = jnp.where(l_rows >= 0, l_rows - me * row_blocks, -1)
    levels = jnp.arange(row_blocks, dtype=jnp.int32)
    hit = local_ids[:, None, :] == levels[None, :, None]
    present = jnp.any(hit, axis=-1)
    slot_of = jnp.sum(jnp.where(hit, jnp.arange(slot_count, dtype=jnp.int32), 0), axis=-1)
    slot_at = jnp.where(present[order], slot_of[order], slot_count)
    table = lower_pos[order][:, None] * (slot_count + 1) + slot_at
    l_pieces = [piece.reshape(slot_count + 1, side, side) for piece in held + swapped]
    return fused_update(table, trailing, pieces, l_pieces)


def solution(mesh):
    placed = (
        P("prow", "pcol"),
        P("pcol", "prow", None),
        P(None, "prow"),
        P("pcol", None, None),
        P("prow", "pcol"),
        P("prow", None),
    )
    return jax.shard_map(
        per_device, mesh=mesh, in_specs=placed, out_specs=P("prow", "pcol"), check_vma=False
    )
```

```python
import functools

import jax
import jax.numpy as jnp
from jax import lax
from jax.experimental import pallas as pl
from jax.experimental.pallas import tpu as pltpu
from jax.sharding import PartitionSpec as P


def _update_kernel(u_starts, n_l, rows, table_ref, trailing_ref, *refs):
    n_u = len(u_starts) - 1
    u_hbm = refs[:n_u]
    l_hbm = refs[n_u:n_u + n_l]
    out_ref = refs[n_u + n_l]
    u_scr, l_scr, lrow, sems = refs[n_u + n_l + 1:]
    side = l_scr.shape[-1]
    held = l_scr.shape[0] // n_l
    step = pl.program_id(0)

    @pl.when(step == 0)
    def _():
        copies = [
            pltpu.make_async_copy(
                u_hbm[j],
                u_scr.at[pl.ds(u_starts[j], u_starts[j + 1] - u_starts[j])],
                sems.at[j],
            )
            for j in range(n_u)
        ] + [
            pltpu.make_async_copy(l_hbm[j], l_scr.at[pl.ds(j * held, held)], sems.at[n_u + j])
            for j in range(n_l)
        ]
        for c in copies:
            c.start()
        for c in copies:
            c.wait()

    groups = rows // side
    panels = lrow.shape[1] // side
    for r in range(groups):
        for p in range(panels):
            idx = table_ref[p, step * groups + r]
            lrow[r * side:(r + 1) * side, p * side:(p + 1) * side] = l_scr[idx]
    tile = 256
    for n in range(out_ref.shape[1] // tile):
        cols = slice(n * tile, (n + 1) * tile)
        acc = jnp.dot(lrow[...], u_scr[:, cols], preferred_element_type=jnp.float32)
        out_ref[:, cols] = (trailing_ref[:, cols].astype(jnp.float32) - acc).astype(out_ref.dtype)


def fused_update(table, trailing, u_pieces, l_pieces):
    rows = 256
    side = l_pieces[0].shape[-1]
    held = l_pieces[0].shape[0]
    n_u, n_l = len(u_pieces), len(l_pieces)
    m, n = trailing.shape
    u_starts = [0]
    for piece in u_pieces:
        u_starts.append(u_starts[-1] + piece.shape[0])
    k = u_starts[-1]
    kernel = functools.partial(_update_kernel, tuple(u_starts), n_l, rows)
    any_spec = pl.BlockSpec(memory_space=pl.ANY)
    grid_spec = pltpu.PrefetchScalarGridSpec(
        num_scalar_prefetch=1,
        grid=(m // rows,),
        in_specs=[pl.BlockSpec((rows, n), lambda g, t: (g, 0))] + [any_spec] * (n_u + n_l),
        out_specs=pl.BlockSpec((rows, n), lambda g, t: (g, 0)),
        scratch_shapes=[
            pltpu.VMEM((k, n), u_pieces[0].dtype),
            pltpu.VMEM((n_l * held, side, side), l_pieces[0].dtype),
            pltpu.VMEM((rows, k), l_pieces[0].dtype),
            pltpu.SemaphoreType.DMA((n_u + n_l,)),
        ],
    )
    return pl.pallas_call(
        kernel,
        grid_spec=grid_spec,
        out_shape=jax.ShapeDtypeStruct((m, n), trailing.dtype),
        compiler_params=pltpu.CompilerParams(
            dimension_semantics=("arbitrary",), vmem_limit_bytes=48 * 1024 * 1024
        ),
        cost_estimate=pl.CostEstimate(
            flops=2 * m * k * n, transcendentals=0, bytes_accessed=2 * (2 * m * n + k * n + n_l * held * side * side)
        ),
    )(table, trailing, *u_pieces, *l_pieces)


def per_device(trailing, lower_slot_blocks, l_rows, d_inv, u_panel, pivot):
    side = d_inv.shape[-1]
    row_blocks = trailing.shape[0] // side
    col_count = trailing.shape[1]
    panels, slot_count = l_rows.shape
    n_rows = lax.axis_size("prow")
    u_own = pivot.shape[0]

    fragments = lower_slot_blocks.reshape(-1, slot_count, side, side)
    scaled = jnp.einsum(
        "ksab,kbc->ksac", fragments, d_inv, preferred_element_type=jnp.float32
    ).astype(jnp.bfloat16)
    scaled = jnp.concatenate([scaled, jnp.zeros_like(scaled[:, :1])], axis=1)
    n_cols = lax.axis_size("pcol")
    col = lax.axis_index("pcol")
    z_step = 4
    crossed = lax.ppermute(scaled, "pcol", [(i, i ^ 2) for i in range(n_cols)])
    held = [scaled, crossed]
    for base in (scaled, crossed):
        for hop in range(1, n_cols // z_step):
            held.append(
                lax.ppermute(
                    base, "pcol", [(i, (i + z_step * hop) % n_cols) for i in range(n_cols)]
                )
            )
    swapped = [lax.ppermute(piece, "pcol", [(i, i ^ 1) for i in range(n_cols)]) for piece in held]

    def lower_sources(c):
        hops = [(c - z_step * hop) % n_cols for hop in range(1, n_cols // z_step)]
        return [c, c ^ 2] + hops + [h ^ 2 for h in hops]

    lower_order = jnp.stack(lower_sources(col) + lower_sources(col ^ 1))
    panel_ids = jnp.arange(panels, dtype=jnp.int32)
    lower_pos = jnp.sum(
        jnp.where(lower_order[None, :] == panel_ids[:, None], panel_ids[None, :], 0), axis=1
    )

    upper_rows = u_panel.reshape(-1, side, col_count)
    lanes = jnp.arange(side, dtype=jnp.int32)
    permuting = (pivot[:, :, None] == lanes[None, None, :]).astype(jnp.bfloat16)
    pivoted = jnp.einsum(
        "kpq,kqn->kpn", permuting, upper_rows, preferred_element_type=jnp.float32
    ).astype(jnp.bfloat16).reshape(-1, col_count)
    me = lax.axis_index("prow")
    x_step = 2

    def shifted(piece, by):
        return lax.ppermute(piece, "prow", [(i, (i + by) % n_rows) for i in range(n_rows)])

    crossed_u = lax.ppermute(pivoted, "prow", [(i, i ^ 1) for i in range(n_rows)])
    pieces = []
    panel_list = []
    for base, flip in ((pivoted, 0), (crossed_u, 1)):
        right = shifted(base, x_step)
        left = shifted(base, -x_step)
        far = shifted(right, x_step) if flip == 0 else shifted(left, -x_step)
        pieces += [base, right, left, far]
        sources = [
            me ^ flip,
            ((me - x_step) % n_rows) ^ flip,
            ((me + x_step) % n_rows) ^ flip,
            ((me + 2 * x_step) % n_rows) ^ flip,
        ]
        for q in sources:
            panel_list += [u_own * q + j for j in range(u_own)]
    order = jnp.stack(panel_list)

    local_ids = jnp.where(l_rows >= 0, l_rows - me * row_blocks, -1)
    levels = jnp.arange(row_blocks, dtype=jnp.int32)
    hit = local_ids[:, None, :] == levels[None, :, None]
    present = jnp.any(hit, axis=-1)
    slot_of = jnp.sum(jnp.where(hit, jnp.arange(slot_count, dtype=jnp.int32), 0), axis=-1)
    slot_at = jnp.where(present[order], slot_of[order], slot_count)
    table = lower_pos[order][:, None] * (slot_count + 1) + slot_at
    l_pieces = [piece.reshape(slot_count + 1, side, side) for piece in held + swapped]
    return fused_update(table, trailing, pieces, l_pieces)


def solution(mesh):
    placed = (
        P("prow", "pcol"),
        P("pcol", "prow", None),
        P(None, "prow"),
        P("pcol", None, None),
        P("prow", "pcol"),
        P("prow", None),
    )
    return jax.shard_map(
        per_device, mesh=mesh, in_specs=placed, out_specs=P("prow", "pcol"), check_vma=False
    )
```

```python
import functools

import jax
import jax.numpy as jnp
from jax import lax
from jax.experimental import pallas as pl
from jax.experimental.pallas import tpu as pltpu
from jax.sharding import PartitionSpec as P


def _update_kernel(u_starts, n_l, rows, table_ref, trailing_ref, *refs):
    n_u = len(u_starts) - 1
    u_hbm = refs[:n_u]
    l_hbm = refs[n_u:n_u + n_l]
    out_ref = refs[n_u + n_l]
    u_scr, l_scr, lrow, sems = refs[n_u + n_l + 1:]
    side = l_scr.shape[-1]
    held = l_scr.shape[0] // n_l
    step = pl.program_id(0)

    @pl.when(step == 0)
    def _():
        copies = [
            pltpu.make_async_copy(
                u_hbm[j],
                u_scr.at[pl.ds(u_starts[j], u_starts[j + 1] - u_starts[j])],
                sems.at[j],
            )
            for j in range(n_u)
        ] + [
            pltpu.make_async_copy(l_hbm[j], l_scr.at[pl.ds(j * held, held)], sems.at[n_u + j])
            for j in range(n_l)
        ]
        for c in copies:
            c.start()
        for c in copies:
            c.wait()

    groups = rows // side
    panels = lrow.shape[1] // side
    for r in range(groups):
        for p in range(panels):
            idx = table_ref[p, step * groups + r]
            lrow[r * side:(r + 1) * side, p * side:(p + 1) * side] = l_scr[idx]
    tile = 256
    for n in range(out_ref.shape[1] // tile):
        cols = slice(n * tile, (n + 1) * tile)
        acc = jnp.dot(lrow[...], u_scr[:, cols], preferred_element_type=jnp.float32)
        out_ref[:, cols] = (trailing_ref[:, cols].astype(jnp.float32) - acc).astype(out_ref.dtype)


def fused_update(table, trailing, u_pieces, l_pieces):
    rows = 256
    side = l_pieces[0].shape[-1]
    held = l_pieces[0].shape[0]
    n_u, n_l = len(u_pieces), len(l_pieces)
    m, n = trailing.shape
    u_starts = [0]
    for piece in u_pieces:
        u_starts.append(u_starts[-1] + piece.shape[0])
    k = u_starts[-1]
    kernel = functools.partial(_update_kernel, tuple(u_starts), n_l, rows)
    any_spec = pl.BlockSpec(memory_space=pl.ANY)
    grid_spec = pltpu.PrefetchScalarGridSpec(
        num_scalar_prefetch=1,
        grid=(m // rows,),
        in_specs=[pl.BlockSpec((rows, n), lambda g, t: (g, 0))] + [any_spec] * (n_u + n_l),
        out_specs=pl.BlockSpec((rows, n), lambda g, t: (g, 0)),
        scratch_shapes=[
            pltpu.VMEM((k, n), u_pieces[0].dtype),
            pltpu.VMEM((n_l * held, side, side), l_pieces[0].dtype),
            pltpu.VMEM((rows, k), l_pieces[0].dtype),
            pltpu.SemaphoreType.DMA((n_u + n_l,)),
        ],
    )
    return pl.pallas_call(
        kernel,
        grid_spec=grid_spec,
        out_shape=jax.ShapeDtypeStruct((m, n), trailing.dtype),
        compiler_params=pltpu.CompilerParams(
            dimension_semantics=("arbitrary",), vmem_limit_bytes=48 * 1024 * 1024
        ),
        cost_estimate=pl.CostEstimate(
            flops=2 * m * k * n, transcendentals=0, bytes_accessed=2 * (2 * m * n + k * n + n_l * held * side * side)
        ),
    )(table, trailing, *u_pieces, *l_pieces)


def per_device(trailing, lower_slot_blocks, l_rows, d_inv, u_panel, pivot):
    side = d_inv.shape[-1]
    row_blocks = trailing.shape[0] // side
    col_count = trailing.shape[1]
    panels, slot_count = l_rows.shape
    n_rows = lax.axis_size("prow")
    u_own = pivot.shape[0]

    fragments = lower_slot_blocks.reshape(-1, slot_count, side, side)
    scaled = jnp.einsum(
        "ksab,kbc->ksac", fragments, d_inv, preferred_element_type=jnp.float32
    ).astype(jnp.bfloat16)
    scaled = jnp.concatenate([scaled, jnp.zeros_like(scaled[:, :1])], axis=1)
    n_cols = lax.axis_size("pcol")
    col = lax.axis_index("pcol")
    z_step = 4
    crossed = lax.ppermute(scaled, "pcol", [(i, i ^ 2) for i in range(n_cols)])
    pair = jnp.concatenate([scaled, crossed], axis=0)
    held = [pair]
    for hop in range(1, n_cols // z_step):
        held.append(
            lax.ppermute(pair, "pcol", [(i, (i + z_step * hop) % n_cols) for i in range(n_cols)])
        )
    swapped = [lax.ppermute(piece, "pcol", [(i, i ^ 1) for i in range(n_cols)]) for piece in held]

    def lower_sources(c):
        found = []
        for hop in range(n_cols // z_step):
            source = (c - z_step * hop) % n_cols
            found += [source, source ^ 2]
        return found

    lower_order = jnp.stack(lower_sources(col) + lower_sources(col ^ 1))
    panel_ids = jnp.arange(panels, dtype=jnp.int32)
    lower_pos = jnp.sum(
        jnp.where(lower_order[None, :] == panel_ids[:, None], panel_ids[None, :], 0), axis=1
    )

    upper_rows = u_panel.reshape(-1, side, col_count)
    lanes = jnp.arange(side, dtype=jnp.int32)
    permuting = (pivot[:, :, None] == lanes[None, None, :]).astype(jnp.bfloat16)
    pivoted = jnp.einsum(
        "kpq,kqn->kpn", permuting, upper_rows, preferred_element_type=jnp.float32
    ).astype(jnp.bfloat16).reshape(-1, col_count)
    me = lax.axis_index("prow")
    x_step = 2

    def shifted(piece, by):
        return lax.ppermute(piece, "prow", [(i, (i + by) % n_rows) for i in range(n_rows)])

    crossed_u = lax.ppermute(pivoted, "prow", [(i, i ^ 1) for i in range(n_rows)])
    pieces = []
    panel_list = []
    for base, flip in ((pivoted, 0), (crossed_u, 1)):
        right = shifted(base, x_step)
        left = shifted(base, -x_step)
        far = shifted(right, x_step) if flip == 0 else shifted(left, -x_step)
        pieces += [base, right, left, far]
        sources = [
            me ^ flip,
            ((me - x_step) % n_rows) ^ flip,
            ((me + x_step) % n_rows) ^ flip,
            ((me + 2 * x_step) % n_rows) ^ flip,
        ]
        for q in sources:
            panel_list += [u_own * q + j for j in range(u_own)]
    order = jnp.stack(panel_list)

    local_ids = jnp.where(l_rows >= 0, l_rows - me * row_blocks, -1)
    levels = jnp.arange(row_blocks, dtype=jnp.int32)
    hit = local_ids[:, None, :] == levels[None, :, None]
    present = jnp.any(hit, axis=-1)
    slot_of = jnp.sum(jnp.where(hit, jnp.arange(slot_count, dtype=jnp.int32), 0), axis=-1)
    slot_at = jnp.where(present[order], slot_of[order], slot_count)
    table = lower_pos[order][:, None] * (slot_count + 1) + slot_at
    l_pieces = [piece.reshape(-1, side, side) for piece in held + swapped]
    return fused_update(table, trailing, pieces, l_pieces)


def solution(mesh):
    placed = (
        P("prow", "pcol"),
        P("pcol", "prow", None),
        P(None, "prow"),
        P("pcol", None, None),
        P("prow", "pcol"),
        P("prow", None),
    )
    return jax.shard_map(
        per_device, mesh=mesh, in_specs=placed, out_specs=P("prow", "pcol"), check_vma=False
    )
```

```python
import functools

import jax
import jax.numpy as jnp
from jax import lax
from jax.experimental import pallas as pl
from jax.experimental.pallas import tpu as pltpu
from jax.sharding import PartitionSpec as P


def _update_kernel(u_starts, n_l, rows, table_ref, base_ref, *refs):
    n_u = len(u_starts) - 1
    u_hbm = refs[:n_u]
    l_hbm = refs[n_u:n_u + n_l]
    out_ref = refs[n_u + n_l]
    u_scr, l_scr, lrow, sems = refs[n_u + n_l + 1:]
    side = l_scr.shape[-1]
    held = l_scr.shape[0] // n_l
    step = pl.program_id(0)

    @pl.when(step == 0)
    def _():
        copies = [
            pltpu.make_async_copy(
                u_hbm[j],
                u_scr.at[pl.ds(u_starts[j], u_starts[j + 1] - u_starts[j])],
                sems.at[j],
            )
            for j in range(n_u)
        ] + [
            pltpu.make_async_copy(l_hbm[j], l_scr.at[pl.ds(j * held, held)], sems.at[n_u + j])
            for j in range(n_l)
        ]
        for c in copies:
            c.start()
        for c in copies:
            c.wait()

    groups = rows // side
    panels = lrow.shape[1] // side
    for r in range(groups):
        for p in range(panels):
            idx = table_ref[p, step * groups + r]
            lrow[r * side:(r + 1) * side, p * side:(p + 1) * side] = l_scr[idx]
    tile = 256
    for n in range(out_ref.shape[1] // tile):
        cols = slice(n * tile, (n + 1) * tile)
        acc = jnp.dot(lrow[...], u_scr[:, cols], preferred_element_type=jnp.float32)
        out_ref[:, cols] = (base_ref[:, cols].astype(jnp.float32) - acc).astype(out_ref.dtype)


def fused_update(table, trailing, u_pieces, l_pieces, out_dtype):
    rows = 256
    side = l_pieces[0].shape[-1]
    held = l_pieces[0].shape[0]
    n_u, n_l = len(u_pieces), len(l_pieces)
    m, n = trailing.shape
    u_starts = [0]
    for piece in u_pieces:
        u_starts.append(u_starts[-1] + piece.shape[0])
    k = u_starts[-1]
    kernel = functools.partial(_update_kernel, tuple(u_starts), n_l, rows)
    any_spec = pl.BlockSpec(memory_space=pl.ANY)
    grid_spec = pltpu.PrefetchScalarGridSpec(
        num_scalar_prefetch=1,
        grid=(m // rows,),
        in_specs=[pl.BlockSpec((rows, n), lambda g, t: (g, 0))] + [any_spec] * (n_u + n_l),
        out_specs=pl.BlockSpec((rows, n), lambda g, t: (g, 0)),
        scratch_shapes=[
            pltpu.VMEM((k, n), u_pieces[0].dtype),
            pltpu.VMEM((n_l * held, side, side), l_pieces[0].dtype),
            pltpu.VMEM((rows, k), l_pieces[0].dtype),
            pltpu.SemaphoreType.DMA((n_u + n_l,)),
        ],
    )
    return pl.pallas_call(
        kernel,
        grid_spec=grid_spec,
        out_shape=jax.ShapeDtypeStruct((m, n), out_dtype),
        compiler_params=pltpu.CompilerParams(
            dimension_semantics=("arbitrary",), vmem_limit_bytes=48 * 1024 * 1024
        ),
        cost_estimate=pl.CostEstimate(
            flops=2 * m * k * n,
            transcendentals=0,
            bytes_accessed=trailing.dtype.itemsize * m * n
            + jnp.dtype(out_dtype).itemsize * m * n
            + 2 * (k * n + n_l * held * side * side),
        ),
    )(table, trailing, *u_pieces, *l_pieces)


def per_device(trailing, lower_slot_blocks, l_rows, d_inv, u_panel, pivot):
    side = d_inv.shape[-1]
    row_blocks = trailing.shape[0] // side
    col_count = trailing.shape[1]
    panels, slot_count = l_rows.shape
    n_rows = lax.axis_size("prow")
    u_own = pivot.shape[0]

    fragments = lower_slot_blocks.reshape(-1, slot_count, side, side)
    scaled = jnp.einsum(
        "ksab,kbc->ksac", fragments, d_inv, preferred_element_type=jnp.float32
    ).astype(jnp.bfloat16)
    scaled = jnp.concatenate([scaled, jnp.zeros_like(scaled[:, :1])], axis=1)
    n_cols = lax.axis_size("pcol")
    col = lax.axis_index("pcol")
    z_step = 4
    crossed = lax.ppermute(scaled, "pcol", [(i, i ^ 2) for i in range(n_cols)])
    held = [scaled, crossed]
    for base in (scaled, crossed):
        for hop in range(1, n_cols // z_step):
            held.append(
                lax.ppermute(
                    base, "pcol", [(i, (i + z_step * hop) % n_cols) for i in range(n_cols)]
                )
            )
    swapped = [lax.ppermute(piece, "pcol", [(i, i ^ 1) for i in range(n_cols)]) for piece in held]

    def lower_sources(c):
        hops = [(c - z_step * hop) % n_cols for hop in range(1, n_cols // z_step)]
        return [c, c ^ 2] + hops + [h ^ 2 for h in hops]

    lower_order = jnp.stack(lower_sources(col) + lower_sources(col ^ 1))
    panel_ids = jnp.arange(panels, dtype=jnp.int32)
    lower_pos = jnp.sum(
        jnp.where(lower_order[None, :] == panel_ids[:, None], panel_ids[None, :], 0), axis=1
    )

    upper_rows = u_panel.reshape(-1, side, col_count)
    lanes = jnp.arange(side, dtype=jnp.int32)
    permuting = (pivot[:, :, None] == lanes[None, None, :]).astype(jnp.bfloat16)
    pivoted = jnp.einsum(
        "kpq,kqn->kpn", permuting, upper_rows, preferred_element_type=jnp.float32
    ).astype(jnp.bfloat16).reshape(-1, col_count)
    me = lax.axis_index("prow")
    x_step = 2

    def shifted(piece, by):
        return lax.ppermute(piece, "prow", [(i, (i + by) % n_rows) for i in range(n_rows)])

    crossed_u = lax.ppermute(pivoted, "prow", [(i, i ^ 1) for i in range(n_rows)])
    pieces, panel_list, late, late_panels = [], [], [], []
    for base, flip in ((pivoted, 0), (crossed_u, 1)):
        right = shifted(base, x_step)
        left = shifted(base, -x_step)
        far = shifted(right, x_step) if flip == 0 else shifted(left, -x_step)
        pieces += [base, right, left]
        late.append(far)
        sources = [
            me ^ flip,
            ((me - x_step) % n_rows) ^ flip,
            ((me + x_step) % n_rows) ^ flip,
        ]
        for q in sources:
            panel_list += [u_own * q + j for j in range(u_own)]
        far_source = ((me + 2 * x_step) % n_rows) ^ flip
        late_panels += [u_own * far_source + j for j in range(u_own)]
    early_count = len(panel_list)
    panel_list += late_panels
    order = jnp.stack(panel_list)

    local_ids = jnp.where(l_rows >= 0, l_rows - me * row_blocks, -1)
    levels = jnp.arange(row_blocks, dtype=jnp.int32)
    hit = local_ids[:, None, :] == levels[None, :, None]
    present = jnp.any(hit, axis=-1)
    slot_of = jnp.sum(jnp.where(hit, jnp.arange(slot_count, dtype=jnp.int32), 0), axis=-1)
    slot_at = jnp.where(present[order], slot_of[order], slot_count)
    table = lower_pos[order][:, None] * (slot_count + 1) + slot_at
    l_pieces = [piece.reshape(-1, side, side) for piece in held + swapped]
    partial = fused_update(table[:early_count], trailing, pieces, l_pieces, jnp.float32)
    return fused_update(table[early_count:], partial, late, l_pieces, trailing.dtype)


def solution(mesh):
    placed = (
        P("prow", "pcol"),
        P("pcol", "prow", None),
        P(None, "prow"),
        P("pcol", None, None),
        P("prow", "pcol"),
        P("prow", None),
    )
    return jax.shard_map(
        per_device, mesh=mesh, in_specs=placed, out_specs=P("prow", "pcol"), check_vma=False
    )
```

```python
import functools

import jax
import jax.numpy as jnp
from jax import lax
from jax.experimental import pallas as pl
from jax.experimental.pallas import tpu as pltpu
from jax.sharding import PartitionSpec as P


def _update_kernel(u_starts, n_l, rows, table_ref, trailing_ref, *refs):
    n_u = len(u_starts) - 1
    u_hbm = refs[:n_u]
    l_hbm = refs[n_u:n_u + n_l]
    out_ref = refs[n_u + n_l]
    u_scr, l_scr, lrow, sems = refs[n_u + n_l + 1:]
    side = l_scr.shape[-1]
    held = l_scr.shape[0] // n_l
    step = pl.program_id(0)

    u_copies = [
        pltpu.make_async_copy(
            u_hbm[j], u_scr.at[pl.ds(u_starts[j], u_starts[j + 1] - u_starts[j])], sems.at[j]
        )
        for j in range(n_u)
    ]
    l_copies = [
        pltpu.make_async_copy(l_hbm[j], l_scr.at[pl.ds(j * held, held)], sems.at[n_u + j])
        for j in range(n_l)
    ]

    @pl.when(step == 0)
    def _():
        for c in l_copies + u_copies:
            c.start()
        for c in l_copies:
            c.wait()

    groups = rows // side
    panels = lrow.shape[1] // side
    for r in range(groups):
        for p in range(panels):
            idx = table_ref[p, step * groups + r]
            lrow[r * side:(r + 1) * side, p * side:(p + 1) * side] = l_scr[idx]

    @pl.when(step == 0)
    def _():
        for c in u_copies:
            c.wait()

    tile = 256
    for n in range(out_ref.shape[1] // tile):
        cols = slice(n * tile, (n + 1) * tile)
        acc = jnp.dot(lrow[...], u_scr[:, cols], preferred_element_type=jnp.float32)
        out_ref[:, cols] = (trailing_ref[:, cols].astype(jnp.float32) - acc).astype(out_ref.dtype)


def fused_update(table, trailing, u_pieces, l_pieces):
    rows = 256
    side = l_pieces[0].shape[-1]
    held = l_pieces[0].shape[0]
    n_u, n_l = len(u_pieces), len(l_pieces)
    m, n = trailing.shape
    u_starts = [0]
    for piece in u_pieces:
        u_starts.append(u_starts[-1] + piece.shape[0])
    k = u_starts[-1]
    kernel = functools.partial(_update_kernel, tuple(u_starts), n_l, rows)
    any_spec = pl.BlockSpec(memory_space=pl.ANY)
    grid_spec = pltpu.PrefetchScalarGridSpec(
        num_scalar_prefetch=1,
        grid=(m // rows,),
        in_specs=[pl.BlockSpec((rows, n), lambda g, t: (g, 0))] + [any_spec] * (n_u + n_l),
        out_specs=pl.BlockSpec((rows, n), lambda g, t: (g, 0)),
        scratch_shapes=[
            pltpu.VMEM((k, n), u_pieces[0].dtype),
            pltpu.VMEM((n_l * held, side, side), l_pieces[0].dtype),
            pltpu.VMEM((rows, k), l_pieces[0].dtype),
            pltpu.SemaphoreType.DMA((n_u + n_l,)),
        ],
    )
    return pl.pallas_call(
        kernel,
        grid_spec=grid_spec,
        out_shape=jax.ShapeDtypeStruct((m, n), trailing.dtype),
        compiler_params=pltpu.CompilerParams(
            dimension_semantics=("arbitrary",), vmem_limit_bytes=48 * 1024 * 1024
        ),
        cost_estimate=pl.CostEstimate(
            flops=2 * m * k * n, transcendentals=0, bytes_accessed=2 * (2 * m * n + k * n + n_l * held * side * side)
        ),
    )(table, trailing, *u_pieces, *l_pieces)


def per_device(trailing, lower_slot_blocks, l_rows, d_inv, u_panel, pivot):
    side = d_inv.shape[-1]
    row_blocks = trailing.shape[0] // side
    col_count = trailing.shape[1]
    panels, slot_count = l_rows.shape
    n_rows = lax.axis_size("prow")
    u_own = pivot.shape[0]

    fragments = lower_slot_blocks.reshape(-1, slot_count, side, side)
    scaled = jnp.einsum(
        "ksab,kbc->ksac", fragments, d_inv, preferred_element_type=jnp.float32
    ).astype(jnp.bfloat16)
    scaled = jnp.concatenate([scaled, jnp.zeros_like(scaled[:, :1])], axis=1)
    upper_rows = u_panel.reshape(-1, side, col_count)
    lanes = jnp.arange(side, dtype=jnp.int32)
    permuting = (pivot[:, :, None] == lanes[None, None, :]).astype(jnp.bfloat16)
    pivoted = jnp.einsum(
        "kpq,kqn->kpn", permuting, upper_rows, preferred_element_type=jnp.float32
    ).astype(jnp.bfloat16).reshape(-1, col_count)
    me = lax.axis_index("prow")
    x_step = 2

    def shifted(piece, by):
        return lax.ppermute(piece, "prow", [(i, (i + by) % n_rows) for i in range(n_rows)])

    crossed_u = lax.ppermute(pivoted, "prow", [(i, i ^ 1) for i in range(n_rows)])
    pieces = []
    panel_list = []
    for base, flip in ((pivoted, 0), (crossed_u, 1)):
        right = shifted(base, x_step)
        left = shifted(base, -x_step)
        far = shifted(right, x_step) if flip == 0 else shifted(left, -x_step)
        pieces += [base, right, left, far]
        sources = [
            me ^ flip,
            ((me - x_step) % n_rows) ^ flip,
            ((me + x_step) % n_rows) ^ flip,
            ((me + 2 * x_step) % n_rows) ^ flip,
        ]
        for q in sources:
            panel_list += [u_own * q + j for j in range(u_own)]
    order = jnp.stack(panel_list)

    n_cols = lax.axis_size("pcol")
    col = lax.axis_index("pcol")
    z_step = 4
    crossed = lax.ppermute(scaled, "pcol", [(i, i ^ 2) for i in range(n_cols)])
    held = [scaled, crossed]
    for base in (scaled, crossed):
        for hop in range(1, n_cols // z_step):
            held.append(
                lax.ppermute(
                    base, "pcol", [(i, (i + z_step * hop) % n_cols) for i in range(n_cols)]
                )
            )
    swapped = [lax.ppermute(piece, "pcol", [(i, i ^ 1) for i in range(n_cols)]) for piece in held]

    def lower_sources(c):
        hops = [(c - z_step * hop) % n_cols for hop in range(1, n_cols // z_step)]
        return [c, c ^ 2] + hops + [h ^ 2 for h in hops]

    lower_order = jnp.stack(lower_sources(col) + lower_sources(col ^ 1))
    panel_ids = jnp.arange(panels, dtype=jnp.int32)
    lower_pos = jnp.sum(
        jnp.where(lower_order[None, :] == panel_ids[:, None], panel_ids[None, :], 0), axis=1
    )

    local_ids = jnp.where(l_rows >= 0, l_rows - me * row_blocks, -1)
    levels = jnp.arange(row_blocks, dtype=jnp.int32)
    hit = local_ids[:, None, :] == levels[None, :, None]
    present = jnp.any(hit, axis=-1)
    slot_of = jnp.sum(jnp.where(hit, jnp.arange(slot_count, dtype=jnp.int32), 0), axis=-1)
    slot_at = jnp.where(present[order], slot_of[order], slot_count)
    table = lower_pos[order][:, None] * (slot_count + 1) + slot_at
    l_pieces = [piece.reshape(slot_count + 1, side, side) for piece in held + swapped]
    return fused_update(table, trailing, pieces, l_pieces)


def solution(mesh):
    placed = (
        P("prow", "pcol"),
        P("pcol", "prow", None),
        P(None, "prow"),
        P("pcol", None, None),
        P("prow", "pcol"),
        P("prow", None),
    )

    return jax.shard_map(
        per_device, mesh=mesh, in_specs=placed, out_specs=P("prow", "pcol"), check_vma=False
    )
```

```python
import functools

import jax
import jax.numpy as jnp
from jax import lax
from jax.experimental import pallas as pl
from jax.experimental.pallas import tpu as pltpu
from jax.sharding import PartitionSpec as P


def _update_kernel(u_starts, n_l, rows, table_ref, trailing_ref, *refs):
    n_u = len(u_starts) - 1
    u_hbm = refs[:n_u]
    l_hbm = refs[n_u:n_u + n_l]
    out_ref = refs[n_u + n_l]
    u_scr, l_scr, lrow, sems, lsems = refs[n_u + n_l + 1:]
    side = l_scr.shape[-1]
    held = l_scr.shape[0] // n_l
    step = pl.program_id(0)

    @pl.when(step == 0)
    def _():
        copies = [
            pltpu.make_async_copy(
                u_hbm[j],
                u_scr.at[pl.ds(u_starts[j], u_starts[j + 1] - u_starts[j])],
                sems.at[j],
            )
            for j in range(n_u)
        ] + [
            pltpu.make_async_copy(l_hbm[j], l_scr.at[pl.ds(j * held, held)], sems.at[n_u + j])
            for j in range(n_l)
        ]
        for c in copies:
            c.start()
        for c in copies:
            c.wait()

    groups = rows // side
    panels = lrow.shape[2] // side
    steps = pl.num_programs(0)

    def assembly(at, slot):
        return [
            pltpu.make_async_copy(
                l_scr.at[table_ref[p, at * groups + r]],
                lrow.at[slot, pl.ds(r * side, side), pl.ds(p * side, side)],
                lsems.at[slot, r * panels + p],
            )
            for r in range(groups)
            for p in range(panels)
        ]

    @pl.when(step == 0)
    def _():
        for c in assembly(0, 0):
            c.start()
        for c in assembly(0, 0):
            c.wait()

    nxt = (step + 1) % 2

    @pl.when(step + 1 < steps)
    def _():
        for c in assembly(step + 1, nxt):
            c.start()

    cur = step % 2
    tile = 256
    for n in range(out_ref.shape[1] // tile):
        cols = slice(n * tile, (n + 1) * tile)
        acc = jnp.dot(lrow[cur], u_scr[:, cols], preferred_element_type=jnp.float32)
        out_ref[:, cols] = (trailing_ref[:, cols].astype(jnp.float32) - acc).astype(out_ref.dtype)

    @pl.when(step + 1 < steps)
    def _():
        for c in assembly(step + 1, nxt):
            c.wait()


def fused_update(table, trailing, u_pieces, l_pieces):
    rows = 512
    side = l_pieces[0].shape[-1]
    held = l_pieces[0].shape[0]
    n_u, n_l = len(u_pieces), len(l_pieces)
    m, n = trailing.shape
    u_starts = [0]
    for piece in u_pieces:
        u_starts.append(u_starts[-1] + piece.shape[0])
    k = u_starts[-1]
    kernel = functools.partial(_update_kernel, tuple(u_starts), n_l, rows)
    any_spec = pl.BlockSpec(memory_space=pl.ANY)
    grid_spec = pltpu.PrefetchScalarGridSpec(
        num_scalar_prefetch=1,
        grid=(m // rows,),
        in_specs=[pl.BlockSpec((rows, n), lambda g, t: (g, 0))] + [any_spec] * (n_u + n_l),
        out_specs=pl.BlockSpec((rows, n), lambda g, t: (g, 0)),
        scratch_shapes=[
            pltpu.VMEM((k, n), u_pieces[0].dtype),
            pltpu.VMEM((n_l * held, side, side), l_pieces[0].dtype),
            pltpu.VMEM((2, rows, k), l_pieces[0].dtype),
            pltpu.SemaphoreType.DMA((n_u + n_l,)),
            pltpu.SemaphoreType.DMA((2, (rows // side) * (k // side))),
        ],
    )
    return pl.pallas_call(
        kernel,
        grid_spec=grid_spec,
        out_shape=jax.ShapeDtypeStruct((m, n), trailing.dtype),
        compiler_params=pltpu.CompilerParams(
            dimension_semantics=("arbitrary",), vmem_limit_bytes=48 * 1024 * 1024
        ),
        cost_estimate=pl.CostEstimate(
            flops=2 * m * k * n, transcendentals=0, bytes_accessed=2 * (2 * m * n + k * n + n_l * held * side * side)
        ),
    )(table, trailing, *u_pieces, *l_pieces)


def per_device(trailing, lower_slot_blocks, l_rows, d_inv, u_panel, pivot):
    side = d_inv.shape[-1]
    row_blocks = trailing.shape[0] // side
    col_count = trailing.shape[1]
    panels, slot_count = l_rows.shape
    n_rows = lax.axis_size("prow")
    u_own = pivot.shape[0]

    fragments = lower_slot_blocks.reshape(-1, slot_count, side, side)
    scaled = jnp.einsum(
        "ksab,kbc->ksac", fragments, d_inv, preferred_element_type=jnp.float32
    ).astype(jnp.bfloat16)
    scaled = jnp.concatenate([scaled, jnp.zeros_like(scaled[:, :1])], axis=1)
    upper_rows = u_panel.reshape(-1, side, col_count)
    lanes = jnp.arange(side, dtype=jnp.int32)
    permuting = (pivot[:, :, None] == lanes[None, None, :]).astype(jnp.bfloat16)
    pivoted = jnp.einsum(
        "kpq,kqn->kpn", permuting, upper_rows, preferred_element_type=jnp.float32
    ).astype(jnp.bfloat16).reshape(-1, col_count)
    me = lax.axis_index("prow")
    x_step = 2

    def shifted(piece, by):
        return lax.ppermute(piece, "prow", [(i, (i + by) % n_rows) for i in range(n_rows)])

    crossed_u = lax.ppermute(pivoted, "prow", [(i, i ^ 1) for i in range(n_rows)])
    pieces = []
    panel_list = []
    for base, flip in ((pivoted, 0), (crossed_u, 1)):
        right = shifted(base, x_step)
        left = shifted(base, -x_step)
        far = shifted(right, x_step) if flip == 0 else shifted(left, -x_step)
        pieces += [base, right, left, far]
        sources = [
            me ^ flip,
            ((me - x_step) % n_rows) ^ flip,
            ((me + x_step) % n_rows) ^ flip,
            ((me + 2 * x_step) % n_rows) ^ flip,
        ]
        for q in sources:
            panel_list += [u_own * q + j for j in range(u_own)]
    order = jnp.stack(panel_list)

    n_cols = lax.axis_size("pcol")
    col = lax.axis_index("pcol")
    z_step = 4
    crossed = lax.ppermute(scaled, "pcol", [(i, i ^ 2) for i in range(n_cols)])
    held = [scaled, crossed]
    for base in (scaled, crossed):
        for hop in range(1, n_cols // z_step):
            held.append(
                lax.ppermute(
                    base, "pcol", [(i, (i + z_step * hop) % n_cols) for i in range(n_cols)]
                )
            )
    swapped = [lax.ppermute(piece, "pcol", [(i, i ^ 1) for i in range(n_cols)]) for piece in held]

    def lower_sources(c):
        hops = [(c - z_step * hop) % n_cols for hop in range(1, n_cols // z_step)]
        return [c, c ^ 2] + hops + [h ^ 2 for h in hops]

    lower_order = jnp.stack(lower_sources(col) + lower_sources(col ^ 1))
    panel_ids = jnp.arange(panels, dtype=jnp.int32)
    lower_pos = jnp.sum(
        jnp.where(lower_order[None, :] == panel_ids[:, None], panel_ids[None, :], 0), axis=1
    )

    local_ids = jnp.where(l_rows >= 0, l_rows - me * row_blocks, -1)
    levels = jnp.arange(row_blocks, dtype=jnp.int32)
    hit = local_ids[:, None, :] == levels[None, :, None]
    present = jnp.any(hit, axis=-1)
    slot_of = jnp.sum(jnp.where(hit, jnp.arange(slot_count, dtype=jnp.int32), 0), axis=-1)
    slot_at = jnp.where(present[order], slot_of[order], slot_count)
    table = lower_pos[order][:, None] * (slot_count + 1) + slot_at
    l_pieces = [piece.reshape(slot_count + 1, side, side) for piece in held + swapped]
    return fused_update(table, trailing, pieces, l_pieces)


def solution(mesh):
    placed = (
        P("prow", "pcol"),
        P("pcol", "prow", None),
        P(None, "prow"),
        P("pcol", None, None),
        P("prow", "pcol"),
        P("prow", None),
    )

    return jax.shard_map(
        per_device, mesh=mesh, in_specs=placed, out_specs=P("prow", "pcol"), check_vma=False
    )
```

```python
import functools

import jax
import jax.numpy as jnp
from jax import lax
from jax.experimental import pallas as pl
from jax.experimental.pallas import tpu as pltpu
from jax.sharding import PartitionSpec as P


def _update_kernel(u_starts, n_l, rows, table_ref, trailing_ref, *refs):
    n_u = len(u_starts) - 1
    u_hbm = refs[:n_u]
    l_hbm = refs[n_u:n_u + n_l]
    out_ref = refs[n_u + n_l]
    u_scr, l_scr, lrow, sems = refs[n_u + n_l + 1:]
    side = l_scr.shape[-1]
    held = (l_scr.shape[0] - 1) // n_l
    step = pl.program_id(0)

    @pl.when(step == 0)
    def _():
        copies = [
            pltpu.make_async_copy(
                u_hbm[j],
                u_scr.at[pl.ds(u_starts[j], u_starts[j + 1] - u_starts[j])],
                sems.at[j],
            )
            for j in range(n_u)
        ] + [
            pltpu.make_async_copy(l_hbm[j], l_scr.at[pl.ds(j * held, held)], sems.at[n_u + j])
            for j in range(n_l)
        ]
        for c in copies:
            c.start()
        l_scr[n_l * held] = jnp.zeros((side, side), l_scr.dtype)
        for c in copies:
            c.wait()

    groups = rows // side
    panels = lrow.shape[1] // side
    for r in range(groups):
        for p in range(panels):
            idx = table_ref[p, step * groups + r]
            lrow[r * side:(r + 1) * side, p * side:(p + 1) * side] = l_scr[idx]
    tile = 256
    for n in range(out_ref.shape[1] // tile):
        cols = slice(n * tile, (n + 1) * tile)
        acc = jnp.dot(lrow[...], u_scr[:, cols], preferred_element_type=jnp.float32)
        out_ref[:, cols] = (trailing_ref[:, cols].astype(jnp.float32) - acc).astype(out_ref.dtype)


def fused_update(table, trailing, u_pieces, l_pieces):
    rows = 1024
    side = l_pieces[0].shape[-1]
    held = l_pieces[0].shape[0]
    n_u, n_l = len(u_pieces), len(l_pieces)
    m, n = trailing.shape
    u_starts = [0]
    for piece in u_pieces:
        u_starts.append(u_starts[-1] + piece.shape[0])
    k = u_starts[-1]
    kernel = functools.partial(_update_kernel, tuple(u_starts), n_l, rows)
    any_spec = pl.BlockSpec(memory_space=pl.ANY)
    grid_spec = pltpu.PrefetchScalarGridSpec(
        num_scalar_prefetch=1,
        grid=(m // rows,),
        in_specs=[pl.BlockSpec((rows, n), lambda g, t: (g, 0))] + [any_spec] * (n_u + n_l),
        out_specs=pl.BlockSpec((rows, n), lambda g, t: (g, 0)),
        scratch_shapes=[
            pltpu.VMEM((k, n), u_pieces[0].dtype),
            pltpu.VMEM((n_l * held + 1, side, side), l_pieces[0].dtype),
            pltpu.VMEM((rows, k), l_pieces[0].dtype),
            pltpu.SemaphoreType.DMA((n_u + n_l,)),
        ],
    )
    return pl.pallas_call(
        kernel,
        grid_spec=grid_spec,
        out_shape=jax.ShapeDtypeStruct((m, n), trailing.dtype),
        compiler_params=pltpu.CompilerParams(
            dimension_semantics=("arbitrary",), vmem_limit_bytes=48 * 1024 * 1024
        ),
        cost_estimate=pl.CostEstimate(
            flops=2 * m * k * n, transcendentals=0, bytes_accessed=2 * (2 * m * n + k * n + n_l * held * side * side)
        ),
    )(table, trailing, *u_pieces, *l_pieces)


def per_device(trailing, lower_slot_blocks, l_rows, d_inv, u_panel, pivot):
    side = d_inv.shape[-1]
    row_blocks = trailing.shape[0] // side
    col_count = trailing.shape[1]
    panels, slot_count = l_rows.shape
    n_rows = lax.axis_size("prow")
    u_own = pivot.shape[0]

    fragments = lower_slot_blocks.reshape(-1, slot_count, side, side)
    scaled = jnp.einsum(
        "ksab,kbc->ksac", fragments, d_inv, preferred_element_type=jnp.float32
    ).astype(jnp.bfloat16)
    upper_rows = u_panel.reshape(-1, side, col_count)
    lanes = jnp.arange(side, dtype=jnp.int32)
    permuting = (pivot[:, :, None] == lanes[None, None, :]).astype(jnp.bfloat16)
    pivoted = jnp.einsum(
        "kpq,kqn->kpn", permuting, upper_rows, preferred_element_type=jnp.float32
    ).astype(jnp.bfloat16).reshape(-1, col_count)
    me = lax.axis_index("prow")
    x_step = 2

    def shifted(piece, by):
        return lax.ppermute(piece, "prow", [(i, (i + by) % n_rows) for i in range(n_rows)])

    crossed_u = lax.ppermute(pivoted, "prow", [(i, i ^ 1) for i in range(n_rows)])
    pieces = []
    panel_list = []
    for base, flip in ((pivoted, 0), (crossed_u, 1)):
        right = shifted(base, x_step)
        left = shifted(base, -x_step)
        far = shifted(right, x_step) if flip == 0 else shifted(left, -x_step)
        pieces += [base, right, left, far]
        sources = [
            me ^ flip,
            ((me - x_step) % n_rows) ^ flip,
            ((me + x_step) % n_rows) ^ flip,
            ((me + 2 * x_step) % n_rows) ^ flip,
        ]
        for q in sources:
            panel_list += [u_own * q + j for j in range(u_own)]
    order = jnp.stack(panel_list)

    n_cols = lax.axis_size("pcol")
    col = lax.axis_index("pcol")
    z_step = 4
    crossed = lax.ppermute(scaled, "pcol", [(i, i ^ 2) for i in range(n_cols)])
    held = [scaled, crossed]
    for base in (scaled, crossed):
        for hop in range(1, n_cols // z_step):
            held.append(
                lax.ppermute(
                    base, "pcol", [(i, (i + z_step * hop) % n_cols) for i in range(n_cols)]
                )
            )
    swapped = [lax.ppermute(piece, "pcol", [(i, i ^ 1) for i in range(n_cols)]) for piece in held]

    def lower_sources(c):
        hops = [(c - z_step * hop) % n_cols for hop in range(1, n_cols // z_step)]
        return [c, c ^ 2] + hops + [h ^ 2 for h in hops]

    lower_order = jnp.stack(lower_sources(col) + lower_sources(col ^ 1))
    panel_ids = jnp.arange(panels, dtype=jnp.int32)
    lower_pos = jnp.sum(
        jnp.where(lower_order[None, :] == panel_ids[:, None], panel_ids[None, :], 0), axis=1
    )

    local_ids = jnp.where(l_rows >= 0, l_rows - me * row_blocks, -1)
    levels = jnp.arange(row_blocks, dtype=jnp.int32)
    hit = local_ids[:, None, :] == levels[None, :, None]
    present = jnp.any(hit, axis=-1)
    slot_of = jnp.sum(jnp.where(hit, jnp.arange(slot_count, dtype=jnp.int32), 0), axis=-1)
    table = jnp.where(
        present[order], lower_pos[order][:, None] * slot_count + slot_of[order], panels * slot_count
    )
    l_pieces = [piece.reshape(-1, side, side) for piece in held + swapped]
    return fused_update(table, trailing, pieces, l_pieces)


def solution(mesh):
    placed = (
        P("prow", "pcol"),
        P("pcol", "prow", None),
        P(None, "prow"),
        P("pcol", None, None),
        P("prow", "pcol"),
        P("prow", None),
    )

    return jax.shard_map(
        per_device, mesh=mesh, in_specs=placed, out_specs=P("prow", "pcol"), check_vma=False
    )
```

```python
import functools

import jax
import jax.numpy as jnp
from jax import lax
from jax.experimental import pallas as pl
from jax.experimental.pallas import tpu as pltpu
from jax.sharding import PartitionSpec as P


def _update_kernel(u_starts, n_l, rows, table_ref, trailing_ref, *refs):
    n_u = len(u_starts) - 1
    u_hbm = refs[:n_u]
    l_hbm = refs[n_u:n_u + n_l]
    out_ref = refs[n_u + n_l]
    u_scr, l_scr, lrow, sems = refs[n_u + n_l + 1:]
    side = l_scr.shape[-1]
    held = (l_scr.shape[0] - 1) // n_l
    step = pl.program_id(0)

    @pl.when(step == 0)
    def _():
        copies = [
            pltpu.make_async_copy(
                u_hbm[j],
                u_scr.at[pl.ds(u_starts[j], u_starts[j + 1] - u_starts[j])],
                sems.at[j],
            )
            for j in range(n_u)
        ] + [
            pltpu.make_async_copy(l_hbm[j], l_scr.at[pl.ds(j * held, held)], sems.at[n_u + j])
            for j in range(n_l)
        ]
        for c in copies:
            c.start()
        l_scr[n_l * held] = jnp.zeros((side, side), l_scr.dtype)
        for c in copies:
            c.wait()

    groups = rows // side
    panels = lrow.shape[1] // side
    for r in range(groups):
        for p in range(panels):
            idx = table_ref[p, step * groups + r]
            lrow[r * side:(r + 1) * side, p * side:(p + 1) * side] = l_scr[idx]
    tile = 256
    for n in range(out_ref.shape[1] // tile):
        cols = slice(n * tile, (n + 1) * tile)
        acc = jnp.dot(lrow[...], u_scr[:, cols], preferred_element_type=jnp.float32)
        out_ref[:, cols] = (trailing_ref[:, cols].astype(jnp.float32) - acc).astype(out_ref.dtype)


def fused_update(table, trailing, u_pieces, l_pieces, out_dtype):
    rows = 512
    side = l_pieces[0].shape[-1]
    held = l_pieces[0].shape[0]
    n_u, n_l = len(u_pieces), len(l_pieces)
    m, n = trailing.shape
    u_starts = [0]
    for piece in u_pieces:
        u_starts.append(u_starts[-1] + piece.shape[0])
    k = u_starts[-1]
    kernel = functools.partial(_update_kernel, tuple(u_starts), n_l, rows)
    any_spec = pl.BlockSpec(memory_space=pl.ANY)
    grid_spec = pltpu.PrefetchScalarGridSpec(
        num_scalar_prefetch=1,
        grid=(m // rows,),
        in_specs=[pl.BlockSpec((rows, n), lambda g, t: (g, 0))] + [any_spec] * (n_u + n_l),
        out_specs=pl.BlockSpec((rows, n), lambda g, t: (g, 0)),
        scratch_shapes=[
            pltpu.VMEM((k, n), u_pieces[0].dtype),
            pltpu.VMEM((n_l * held + 1, side, side), l_pieces[0].dtype),
            pltpu.VMEM((rows, k), l_pieces[0].dtype),
            pltpu.SemaphoreType.DMA((n_u + n_l,)),
        ],
    )
    return pl.pallas_call(
        kernel,
        grid_spec=grid_spec,
        out_shape=jax.ShapeDtypeStruct((m, n), out_dtype),
        compiler_params=pltpu.CompilerParams(
            dimension_semantics=("arbitrary",), vmem_limit_bytes=48 * 1024 * 1024
        ),
        cost_estimate=pl.CostEstimate(
            flops=2 * m * k * n,
            transcendentals=0,
            bytes_accessed=trailing.dtype.itemsize * m * n
            + jnp.dtype(out_dtype).itemsize * m * n
            + 2 * (k * n + n_l * held * side * side),
        ),
    )(table, trailing, *u_pieces, *l_pieces)


def per_device(trailing, lower_slot_blocks, l_rows, d_inv, u_panel, pivot):
    side = d_inv.shape[-1]
    row_blocks = trailing.shape[0] // side
    col_count = trailing.shape[1]
    panels, slot_count = l_rows.shape
    n_rows = lax.axis_size("prow")
    u_own = pivot.shape[0]

    fragments = lower_slot_blocks.reshape(-1, slot_count, side, side)
    scaled = jnp.einsum(
        "ksab,kbc->ksac", fragments, d_inv, preferred_element_type=jnp.float32
    ).astype(jnp.bfloat16)
    upper_rows = u_panel.reshape(-1, side, col_count)
    lanes = jnp.arange(side, dtype=jnp.int32)
    permuting = (pivot[:, :, None] == lanes[None, None, :]).astype(jnp.bfloat16)
    pivoted = jnp.einsum(
        "kpq,kqn->kpn", permuting, upper_rows, preferred_element_type=jnp.float32
    ).astype(jnp.bfloat16).reshape(-1, col_count)
    me = lax.axis_index("prow")
    x_step = 2

    def shifted(piece, by):
        return lax.ppermute(piece, "prow", [(i, (i + by) % n_rows) for i in range(n_rows)])

    crossed_u = lax.ppermute(pivoted, "prow", [(i, i ^ 1) for i in range(n_rows)])
    pieces, panel_list, late, late_panels = [], [], [], []
    for base, flip in ((pivoted, 0), (crossed_u, 1)):
        right = shifted(base, x_step)
        left = shifted(base, -x_step)
        far = shifted(right, x_step) if flip == 0 else shifted(left, -x_step)
        pieces += [base, right, left]
        late.append(far)
        sources = [
            me ^ flip,
            ((me - x_step) % n_rows) ^ flip,
            ((me + x_step) % n_rows) ^ flip,
        ]
        for q in sources:
            panel_list += [u_own * q + j for j in range(u_own)]
        far_source = ((me + 2 * x_step) % n_rows) ^ flip
        late_panels += [u_own * far_source + j for j in range(u_own)]
    early_count = len(panel_list)
    panel_list += late_panels
    order = jnp.stack(panel_list)

    n_cols = lax.axis_size("pcol")
    col = lax.axis_index("pcol")
    z_step = 4
    crossed = lax.ppermute(scaled, "pcol", [(i, i ^ 2) for i in range(n_cols)])
    held = [scaled, crossed]
    for base in (scaled, crossed):
        for hop in range(1, n_cols // z_step):
            held.append(
                lax.ppermute(
                    base, "pcol", [(i, (i + z_step * hop) % n_cols) for i in range(n_cols)]
                )
            )
    swapped = [lax.ppermute(piece, "pcol", [(i, i ^ 1) for i in range(n_cols)]) for piece in held]

    def lower_sources(c):
        hops = [(c - z_step * hop) % n_cols for hop in range(1, n_cols // z_step)]
        return [c, c ^ 2] + hops + [h ^ 2 for h in hops]

    lower_order = jnp.stack(lower_sources(col) + lower_sources(col ^ 1))
    panel_ids = jnp.arange(panels, dtype=jnp.int32)
    lower_pos = jnp.sum(
        jnp.where(lower_order[None, :] == panel_ids[:, None], panel_ids[None, :], 0), axis=1
    )

    local_ids = jnp.where(l_rows >= 0, l_rows - me * row_blocks, -1)
    levels = jnp.arange(row_blocks, dtype=jnp.int32)
    hit = local_ids[:, None, :] == levels[None, :, None]
    present = jnp.any(hit, axis=-1)
    slot_of = jnp.sum(jnp.where(hit, jnp.arange(slot_count, dtype=jnp.int32), 0), axis=-1)
    table = jnp.where(
        present[order], lower_pos[order][:, None] * slot_count + slot_of[order], panels * slot_count
    )
    l_pieces = [piece.reshape(-1, side, side) for piece in held + swapped]
    partial = fused_update(table[:early_count], trailing, pieces, l_pieces, jnp.float32)
    return fused_update(table[early_count:], partial, late, l_pieces, trailing.dtype)


def solution(mesh):
    placed = (
        P("prow", "pcol"),
        P("pcol", "prow", None),
        P(None, "prow"),
        P("pcol", None, None),
        P("prow", "pcol"),
        P("prow", None),
    )

    return jax.shard_map(
        per_device, mesh=mesh, in_specs=placed, out_specs=P("prow", "pcol"), check_vma=False
    )
```

```python
import functools

import jax
import jax.numpy as jnp
from jax import lax
from jax.experimental import pallas as pl
from jax.experimental.pallas import tpu as pltpu
from jax.sharding import PartitionSpec as P


def _update_kernel(u_starts, n_l, rows, late, table_ref, trailing_ref, *refs):
    n_u = len(u_starts) - 1
    u_hbm = refs[:n_u]
    l_hbm = refs[n_u:n_u + n_l]
    out_ref, late_ref = refs[n_u + n_l:n_u + n_l + 2]
    u_scr, l_scr, lrow, sems = refs[n_u + n_l + 2:]
    side = l_scr.shape[-1]
    held = (l_scr.shape[0] - 1) // n_l
    step = pl.program_id(0)

    @pl.when(step == 0)
    def _():
        copies = [
            pltpu.make_async_copy(
                u_hbm[j],
                u_scr.at[pl.ds(u_starts[j], u_starts[j + 1] - u_starts[j])],
                sems.at[j],
            )
            for j in range(n_u)
        ] + [
            pltpu.make_async_copy(l_hbm[j], l_scr.at[pl.ds(j * held, held)], sems.at[n_u + j])
            for j in range(n_l)
        ]
        for c in copies:
            c.start()
        l_scr[n_l * held] = jnp.zeros((side, side), l_scr.dtype)
        for c in copies:
            c.wait()

    groups = rows // side
    panels = lrow.shape[1] // side
    for r in range(groups):
        for p in range(panels):
            idx = table_ref[p, step * groups + r]
            lrow[r * side:(r + 1) * side, p * side:(p + 1) * side] = l_scr[idx]
        for p in range(late):
            idx = table_ref[panels + p, step * groups + r]
            late_ref[r * side:(r + 1) * side, p * side:(p + 1) * side] = l_scr[idx]
    tile = 256
    for n in range(out_ref.shape[1] // tile):
        cols = slice(n * tile, (n + 1) * tile)
        acc = jnp.dot(lrow[...], u_scr[:, cols], preferred_element_type=jnp.float32)
        out_ref[:, cols] = (trailing_ref[:, cols].astype(jnp.float32) - acc).astype(out_ref.dtype)


def fused_update(table, trailing, u_pieces, l_pieces, late):
    rows = 512
    side = l_pieces[0].shape[-1]
    held = l_pieces[0].shape[0]
    n_u, n_l = len(u_pieces), len(l_pieces)
    m, n = trailing.shape
    u_starts = [0]
    for piece in u_pieces:
        u_starts.append(u_starts[-1] + piece.shape[0])
    k = u_starts[-1]
    kernel = functools.partial(_update_kernel, tuple(u_starts), n_l, rows, late)
    any_spec = pl.BlockSpec(memory_space=pl.ANY)
    grid_spec = pltpu.PrefetchScalarGridSpec(
        num_scalar_prefetch=1,
        grid=(m // rows,),
        in_specs=[pl.BlockSpec((rows, n), lambda g, t: (g, 0))] + [any_spec] * (n_u + n_l),
        out_specs=[
            pl.BlockSpec((rows, n), lambda g, t: (g, 0)),
            pl.BlockSpec((rows, late * side), lambda g, t: (g, 0)),
        ],
        scratch_shapes=[
            pltpu.VMEM((k, n), u_pieces[0].dtype),
            pltpu.VMEM((n_l * held + 1, side, side), l_pieces[0].dtype),
            pltpu.VMEM((rows, k), l_pieces[0].dtype),
            pltpu.SemaphoreType.DMA((n_u + n_l,)),
        ],
    )
    return pl.pallas_call(
        kernel,
        grid_spec=grid_spec,
        out_shape=(
            jax.ShapeDtypeStruct((m, n), jnp.float32),
            jax.ShapeDtypeStruct((m, late * side), l_pieces[0].dtype),
        ),
        compiler_params=pltpu.CompilerParams(
            dimension_semantics=("arbitrary",), vmem_limit_bytes=48 * 1024 * 1024
        ),
        cost_estimate=pl.CostEstimate(
            flops=2 * m * k * n,
            transcendentals=0,
            bytes_accessed=2 * m * n + 4 * m * n + 2 * (k * n + n_l * held * side * side),
        ),
    )(table, trailing, *u_pieces, *l_pieces)


def _finish_kernel(partial_ref, lower_ref, *refs):
    u_refs, out_ref = refs[:-1], refs[-1]
    depth = u_refs[0].shape[0]
    tile = 256
    for n in range(out_ref.shape[1] // tile):
        cols = slice(n * tile, (n + 1) * tile)
        acc = partial_ref[:, cols]
        for j, u_ref in enumerate(u_refs):
            acc = acc - jnp.dot(
                lower_ref[:, j * depth:(j + 1) * depth],
                u_ref[:, cols],
                preferred_element_type=jnp.float32,
            )
        out_ref[:, cols] = acc.astype(out_ref.dtype)


def finish_update(partial, lower, u_pieces, out_dtype):
    rows = 512
    m, n = partial.shape
    k = lower.shape[1]
    return pl.pallas_call(
        _finish_kernel,
        grid=(m // rows,),
        in_specs=[
            pl.BlockSpec((rows, n), lambda g: (g, 0)),
            pl.BlockSpec((rows, k), lambda g: (g, 0)),
        ]
        + [pl.BlockSpec(piece.shape, lambda g: (0, 0)) for piece in u_pieces],
        out_specs=pl.BlockSpec((rows, n), lambda g: (g, 0)),
        out_shape=jax.ShapeDtypeStruct((m, n), out_dtype),
        compiler_params=pltpu.CompilerParams(
            dimension_semantics=("arbitrary",), vmem_limit_bytes=60 * 1024 * 1024
        ),
        cost_estimate=pl.CostEstimate(
            flops=2 * m * k * n, transcendentals=0, bytes_accessed=4 * m * n + 2 * (m * n + m * k + k * n)
        ),
    )(partial, lower, *u_pieces)


def per_device(trailing, lower_slot_blocks, l_rows, d_inv, u_panel, pivot):
    side = d_inv.shape[-1]
    row_blocks = trailing.shape[0] // side
    col_count = trailing.shape[1]
    panels, slot_count = l_rows.shape
    n_rows = lax.axis_size("prow")
    u_own = pivot.shape[0]

    fragments = lower_slot_blocks.reshape(-1, slot_count, side, side)
    scaled = jnp.einsum(
        "ksab,kbc->ksac", fragments, d_inv, preferred_element_type=jnp.float32
    ).astype(jnp.bfloat16)
    upper_rows = u_panel.reshape(-1, side, col_count)
    lanes = jnp.arange(side, dtype=jnp.int32)
    permuting = (pivot[:, :, None] == lanes[None, None, :]).astype(jnp.bfloat16)
    pivoted = jnp.einsum(
        "kpq,kqn->kpn", permuting, upper_rows, preferred_element_type=jnp.float32
    ).astype(jnp.bfloat16).reshape(-1, col_count)
    me = lax.axis_index("prow")
    x_step = 2

    def shifted(piece, by):
        return lax.ppermute(piece, "prow", [(i, (i + by) % n_rows) for i in range(n_rows)])

    crossed_u = lax.ppermute(pivoted, "prow", [(i, i ^ 1) for i in range(n_rows)])
    pieces, panel_list, late, late_panels = [], [], [], []
    for base, flip in ((pivoted, 0), (crossed_u, 1)):
        right = shifted(base, x_step)
        left = shifted(base, -x_step)
        far = shifted(right, x_step) if flip == 0 else shifted(left, -x_step)
        pieces += [base, right, left]
        late.append(far)
        sources = [
            me ^ flip,
            ((me - x_step) % n_rows) ^ flip,
            ((me + x_step) % n_rows) ^ flip,
        ]
        for q in sources:
            panel_list += [u_own * q + j for j in range(u_own)]
        far_source = ((me + 2 * x_step) % n_rows) ^ flip
        late_panels += [u_own * far_source + j for j in range(u_own)]
    early_count = len(panel_list)
    panel_list += late_panels
    order = jnp.stack(panel_list)

    n_cols = lax.axis_size("pcol")
    col = lax.axis_index("pcol")
    z_step = 4
    crossed = lax.ppermute(scaled, "pcol", [(i, i ^ 2) for i in range(n_cols)])
    held = [scaled, crossed]
    for base in (scaled, crossed):
        for hop in range(1, n_cols // z_step):
            held.append(
                lax.ppermute(
                    base, "pcol", [(i, (i + z_step * hop) % n_cols) for i in range(n_cols)]
                )
            )
    swapped = [lax.ppermute(piece, "pcol", [(i, i ^ 1) for i in range(n_cols)]) for piece in held]

    def lower_sources(c):
        hops = [(c - z_step * hop) % n_cols for hop in range(1, n_cols // z_step)]
        return [c, c ^ 2] + hops + [h ^ 2 for h in hops]

    lower_order = jnp.stack(lower_sources(col) + lower_sources(col ^ 1))
    panel_ids = jnp.arange(panels, dtype=jnp.int32)
    lower_pos = jnp.sum(
        jnp.where(lower_order[None, :] == panel_ids[:, None], panel_ids[None, :], 0), axis=1
    )

    local_ids = jnp.where(l_rows >= 0, l_rows - me * row_blocks, -1)
    levels = jnp.arange(row_blocks, dtype=jnp.int32)
    hit = local_ids[:, None, :] == levels[None, :, None]
    present = jnp.any(hit, axis=-1)
    slot_of = jnp.sum(jnp.where(hit, jnp.arange(slot_count, dtype=jnp.int32), 0), axis=-1)
    table = jnp.where(
        present[order], lower_pos[order][:, None] * slot_count + slot_of[order], panels * slot_count
    )
    l_pieces = [piece.reshape(-1, side, side) for piece in held + swapped]
    partial, late_lower = fused_update(
        table, trailing, pieces, l_pieces, (len(panel_list) - early_count)
    )
    return finish_update(partial, late_lower, late, trailing.dtype)


def solution(mesh):
    placed = (
        P("prow", "pcol"),
        P("pcol", "prow", None),
        P(None, "prow"),
        P("pcol", None, None),
        P("prow", "pcol"),
        P("prow", None),
    )

    return jax.shard_map(
        per_device, mesh=mesh, in_specs=placed, out_specs=P("prow", "pcol"), check_vma=False
    )
```
